512 devices in a mesh: leaf: 8 (over y_hi, x), level: 64 (over y_lo, z, core).
Axes of the slice: x: 4, y: 4 (y_hi: 2, y_lo: 2; y = y_hi * 2 + y_lo), z: 16, core: 2. Of those that a mesh axis runs over, the one named last changes fastest.
Arguments:
- points: bfloat16 [524288, 64], P(('leaf', 'level')), may hold values from -1.6953125 to 1.6953125
- sketch_matrix: bfloat16 [524288, 64], P(('leaf', 'level')), may hold values from -6 to 6
- leaf_order: int32 [512, 1024], P(('leaf', 'level')), may hold values from 0 to 1023, each once within a row
Outputs:
- products: float32 [524288, 256], P(('leaf', 'level'))
- gram_out: float32 [512, 4, 64, 64], P(('leaf', 'level'))
The draws below stay inside these ranges and needn't reach their ends.
Inputs may be any that keep to these rules, and one draw needn't show every extreme that they name: `leaf_order`: each row is a permutation of 0 to 1023.
All inputs are finite; a program needn't handle non-finite values.
Results may differ from the reference program's by a relative error of at most 0.0029.
Values may be sent and summed in bfloat16 or wider, within the bound.
No kernel may reach another device: no remote copies, remote signals or barrier semaphores. Data moves between devices by JAX's collectives and lax.ppermute only.
A program may use at most 64 MiB of HBM per device.

```python
import math
import jax
import jax.numpy as jnp
import numpy as np
from jax import lax

DIM = 64
RANK = 64
PTS_DEV = 1024
TIERS = 4
NPTS = 524288
N_LEAF = 8
N_LEVEL = 64


def block_levels(stream_key, shape, split, least, top_value):
    level = 1.0
    for dim, shards_of in split:
        heights = jax.random.uniform(jax.random.fold_in(jax.random.fold_in(stream_key, 6), dim), (shards_of,), jnp.float32, least / len(split), top_value / len(split))
        level = level * jnp.repeat(jnp.exp(heights), shape[dim] // shards_of).reshape((-1,) + (1,) * (len(shape) - 1 - dim))
    return level


def bell_draw(key, dims, deviation, reach, shards=(), kind=jnp.bfloat16):
    result = deviation * jax.random.normal(key, dims, jnp.float32)
    if shards:
        result = result * block_levels(key, dims, shards, -0.22, 0.18)
    return jnp.clip(result, -reach, reach).astype(kind)


def setup_inputs(seed: int = 0) -> dict:
    streams_of = jax.random.split(jax.random.key(seed), 4)
    return {
        "points": jnp.clip(jax.random.uniform(streams_of[0], (NPTS, DIM), jnp.float32, -1.6953125, 1.6953125) * block_levels(streams_of[0], (NPTS, DIM), ((0, 512),), -0.4, 0.0), -1.6953125, 1.6953125).astype(jnp.bfloat16),
        "sketch_matrix": bell_draw(streams_of[1], (NPTS, RANK), 1.0, 6.0, ((0, 512),)),
        "leaf_order": jax.vmap(lambda own: jax.random.permutation(own, PTS_DEV))(jax.random.split(streams_of[2], (N_LEAF * N_LEVEL))).reshape((N_LEAF * N_LEVEL, PTS_DEV)).astype(jnp.int32),
    }


def kernel_product(row_pts, col_pts, col_sketch, width):
    row_sq = lax.optimization_barrier(jnp.sum(jnp.square(row_pts.astype(jnp.float32)), axis=-1))
    col_sq = lax.optimization_barrier(jnp.sum(jnp.square(col_pts.astype(jnp.float32)), axis=-1))
    cross = lax.dot_general(row_pts, col_pts, (((1,), (1,)), ((), ())), preferred_element_type=jnp.float32)
    distance = row_sq[:, None] + col_sq[None, :] - 2.0 * cross
    kernel = jnp.exp((2.0 * width - distance) * (2.0 / width)).astype(jnp.bfloat16)
    return jnp.dot(kernel, col_sketch, preferred_element_type=jnp.float32)

def reference(points, sketch_matrix, leaf_order):
    located = points.reshape(N_LEAF * N_LEVEL, PTS_DEV, DIM)
    located = jnp.take_along_axis(located, leaf_order.astype(jnp.int32)[:, :, None], axis=1)
    located = located.reshape(N_LEAF, N_LEVEL, PTS_DEV, DIM)
    sketches = sketch_matrix.reshape(N_LEAF, N_LEVEL, PTS_DEV, RANK)
    leaf_bits = TIERS - 1
    tables = []
    for tier_num in range(leaf_bits):
        half_size = 1 << tier_num
        listing = [[(leaf_num >> tier_num ^ 1) << tier_num | inner for inner in range(half_size)] for leaf_num in range(N_LEAF)]
        tables.append(jnp.asarray(np.array(listing, dtype=np.int32)))

    def per_device(device_num):
        leaf_num = device_num // N_LEVEL
        block_num = device_num % N_LEVEL
        row_pts = located[leaf_num, block_num]
        results = []
        for tier_num in range(leaf_bits):
            sib_ids = tables[tier_num][leaf_num]
            col_pts = located[sib_ids, block_num].reshape(-1, DIM)
            col_sketch = sketches[sib_ids, block_num].reshape(-1, RANK)
            results.append(kernel_product(row_pts, col_pts, col_sketch, DIM) / math.sqrt(col_pts.shape[0]))
        partner = block_num + 1 - 2 * (block_num % 2)
        col_pts = located[:, partner].reshape(-1, DIM)
        col_sketch = sketches[:, partner].reshape(-1, RANK)
        results.append(kernel_product(row_pts, col_pts, col_sketch, DIM) / math.sqrt(col_pts.shape[0]))
        return jnp.concatenate(results, axis=-1)
    products = lax.map(per_device, jnp.arange(N_LEAF * N_LEVEL, dtype=jnp.int32))
    tiers_view = products.reshape(N_LEAF, N_LEVEL, PTS_DEV, TIERS, RANK)
    grams = []
    for tier_num in range(TIERS):
        piece = tiers_view[:, :, :, tier_num, :]
        local = jnp.einsum('abpi,abpj->abij', piece, piece, precision=lax.Precision.HIGHEST)
        group = 1 << tier_num
        summed = local.reshape(N_LEAF // group, group, N_LEVEL, RANK, RANK).sum(axis=1, keepdims=True)
        summed = jnp.broadcast_to(summed, (N_LEAF // group, group, N_LEVEL, RANK, RANK)).reshape(N_LEAF, N_LEVEL, RANK, RANK)
        grams.append(summed / (group * PTS_DEV))
    gram_out = jnp.stack(grams, axis=2).reshape(N_LEAF * N_LEVEL, TIERS, RANK, RANK)
    return (products.reshape(N_LEAF * N_LEVEL * PTS_DEV, TIERS * RANK), gram_out)
```

```python
import math

import jax
import jax.numpy as jnp
from jax import lax
from jax.sharding import Mesh, PartitionSpec as P


def squares_of(coords):
    return jnp.sum(jnp.square(coords.astype(jnp.float32)), axis=-1)


def tier_product(row_pts, row_sq, cols, dim):
    col_pts = cols[:, :dim]
    col_sketch = cols[:, dim:]
    col_sq = squares_of(col_pts)
    cross = lax.dot_general(
        row_pts, col_pts, (((1,), (1,)), ((), ())), preferred_element_type=jnp.float32
    )
    distance = row_sq[:, None] + col_sq[None, :] - 2.0 * cross
    kernel = jnp.exp((2.0 * dim - distance) * (2.0 / dim)).astype(jnp.bfloat16)
    out = jnp.dot(kernel, col_sketch, preferred_element_type=jnp.float32)
    return out / math.sqrt(cols.shape[0])


def per_device(points, sketch_matrix, leaf_order):
    dim = points.shape[1]
    located = jnp.take(points, leaf_order[0], axis=0)
    rows_n = located.shape[0]
    row_sq = squares_of(located)
    packed = jnp.concatenate([located, sketch_matrix], axis=1)
    n_leaf = lax.axis_size("leaf")
    leaf_bits = n_leaf.bit_length() - 1
    gathered = lax.all_gather(packed, ("leaf", "pair"))
    blocks = gathered.reshape(n_leaf, 2, rows_n, packed.shape[1])
    leaf_pos = lax.axis_index("leaf")
    pair_pos = lax.axis_index("pair")
    near = lax.dynamic_index_in_dim(blocks, pair_pos, axis=1, keepdims=False)
    far = lax.dynamic_index_in_dim(blocks, 1 - pair_pos, axis=1, keepdims=False)
    results = []
    for tier_num in range(leaf_bits):
        half = 1 << tier_num
        start = ((leaf_pos >> tier_num) ^ 1) << tier_num
        sib = lax.dynamic_slice_in_dim(near, start, half, axis=0)
        results.append(tier_product(located, row_sq, sib.reshape(half * rows_n, -1), dim))
    results.append(tier_product(located, row_sq, far.reshape(n_leaf * rows_n, -1), dim))
    partial_grams = jnp.stack(
        [
            jnp.dot(p.T, p, precision=lax.Precision.HIGHEST, preferred_element_type=jnp.float32)
            for p in results
        ]
    )
    all_grams = lax.all_gather(partial_grams[1:], "leaf")
    leaf_ids = jnp.arange(n_leaf, dtype=jnp.int32)
    summed = [partial_grams[0]]
    for tier_num in range(1, len(results)):
        member = (leaf_ids >> tier_num) == (leaf_pos >> tier_num)
        picked = jnp.where(member[:, None, None], all_grams[:, tier_num - 1], 0.0)
        summed.append(jnp.sum(picked, axis=0))
    stacked = jnp.stack(summed)
    divisors = jnp.asarray(
        [float((1 << tier_num) * rows_n) for tier_num in range(len(results))], jnp.float32
    )
    stacked = stacked / divisors[:, None, None]
    return (jnp.concatenate(results, axis=1), stacked[None])


def solution(mesh):
    n_leaf = mesh.shape["leaf"]
    n_level = mesh.shape["level"]
    fine = Mesh(mesh.devices.reshape(n_leaf, n_level // 2, 2), ("leaf", "lvl", "pair"))
    axes = ("leaf", "lvl", "pair")
    in_specs = (P(axes, None), P(axes, None), P(axes, None))
    out_specs = (P(axes, None), P(axes, None, None, None))
    return jax.shard_map(
        per_device, mesh=fine, in_specs=in_specs, out_specs=out_specs, check_vma=False
    )
```

```python
import math

import jax
import jax.numpy as jnp
from jax import lax
from jax.sharding import Mesh, PartitionSpec as P


def swapped(value, axis, stride):
    mask = 2**stride
    pairs = [(source, source ^ mask) for source in range(lax.axis_size(axis))]
    return lax.ppermute(value, axis, pairs)


def squares_of(coords):
    return jnp.sum(jnp.square(coords.astype(jnp.float32)), axis=-1)


def raw_product(row_pts, row_sq, cols, dim):
    col_pts = cols[:, :dim]
    col_sketch = cols[:, dim:]
    col_sq = squares_of(col_pts)
    cross = lax.dot_general(
        row_pts, col_pts, (((1,), (1,)), ((), ())), preferred_element_type=jnp.float32
    )
    distance = row_sq[:, None] + col_sq[None, :] - 2.0 * cross
    kernel = jnp.exp((2.0 * dim - distance) * (2.0 / dim)).astype(jnp.bfloat16)
    return jnp.dot(kernel, col_sketch, preferred_element_type=jnp.float32)


def gram_of(product):
    return jnp.dot(
        product.T, product, precision=lax.Precision.HIGHEST, preferred_element_type=jnp.float32
    )


def per_device(points, sketch_matrix, leaf_order):
    dim = points.shape[1]
    located = jnp.take(points, leaf_order[0], axis=0)
    rows_n = located.shape[0]
    row_sq = squares_of(located)
    packed = jnp.concatenate([located, sketch_matrix], axis=1)
    leaf_bits = lax.axis_size("leaf").bit_length() - 1
    far_pieces = [swapped(packed, "pair", 0)]
    cluster = packed
    results = []
    grams = []
    for tier_num in range(leaf_bits):
        sib = swapped(cluster, "leaf", tier_num)
        far_pieces.append(swapped(sib, "pair", 0))
        product = raw_product(located, row_sq, sib, dim) / math.sqrt(sib.shape[0])
        results.append(product)
        local = gram_of(product)
        for bit_num in range(tier_num):
            local = local + swapped(local, "leaf", bit_num)
        grams.append(local)
        cluster = jnp.concatenate([cluster, sib])
    far_total = None
    far_rows = 0
    for piece in far_pieces:
        part = raw_product(located, row_sq, piece, dim)
        far_total = part if far_total is None else far_total + part
        far_rows += piece.shape[0]
    product = far_total / math.sqrt(far_rows)
    results.append(product)
    local = gram_of(product)
    for bit_num in range(leaf_bits):
        local = local + swapped(local, "leaf", bit_num)
    grams.append(local)
    stacked = jnp.stack(grams)
    divisors = jnp.asarray(
        [float((1 << tier_num) * rows_n) for tier_num in range(len(grams))], jnp.float32
    )
    stacked = stacked / divisors[:, None, None]
    return (jnp.concatenate(results, axis=1), stacked[None])


def solution(mesh):
    n_leaf = mesh.shape["leaf"]
    n_level = mesh.shape["level"]
    fine = Mesh(mesh.devices.reshape(n_leaf, n_level // 2, 2), ("leaf", "lvl", "pair"))
    axes = ("leaf", "lvl", "pair")
    in_specs = (P(axes, None), P(axes, None), P(axes, None))
    out_specs = (P(axes, None), P(axes, None, None, None))
    return jax.shard_map(
        per_device, mesh=fine, in_specs=in_specs, out_specs=out_specs, check_vma=False
    )
```

```python
import math

import jax
import jax.numpy as jnp
from jax import lax
from jax.sharding import Mesh, PartitionSpec as P


def swapped(value, axis, stride):
    mask = 2**stride
    pairs = [(source, source ^ mask) for source in range(lax.axis_size(axis))]
    return lax.ppermute(value, axis, pairs)


def squares_of(coords):
    return jnp.sum(jnp.square(coords.astype(jnp.float32)), axis=-1)


def raw_product(row_pts, row_sq, cols, dim):
    col_pts = cols[:, :dim]
    col_sketch = cols[:, dim:]
    col_sq = squares_of(col_pts)
    cross = lax.dot_general(
        row_pts, col_pts, (((1,), (1,)), ((), ())), preferred_element_type=jnp.float32
    )
    distance = row_sq[:, None] + col_sq[None, :] - 2.0 * cross
    kernel = jnp.exp((2.0 * dim - distance) * (2.0 / dim)).astype(jnp.bfloat16)
    return jnp.dot(kernel, col_sketch, preferred_element_type=jnp.float32)


def gram_of(product):
    return jnp.dot(
        product.T, product, precision=lax.Precision.HIGHEST, preferred_element_type=jnp.float32
    )


def per_device(points, sketch_matrix, leaf_order):
    dim = points.shape[1]
    rows_n = points.shape[0]
    picks = leaf_order[0][:, None] == jnp.arange(rows_n, dtype=leaf_order.dtype)[None, :]
    located = jnp.dot(
        picks.astype(points.dtype), points, preferred_element_type=jnp.float32
    ).astype(points.dtype)
    row_sq = squares_of(located)
    packed = jnp.concatenate([located, sketch_matrix], axis=1)
    leaf_bits = lax.axis_size("leaf").bit_length() - 1
    far_pieces = []
    cluster = packed
    results = []
    grams = []
    for tier_num in range(leaf_bits):
        sib = swapped(cluster, "leaf", tier_num)
        if tier_num == 0:
            far_pieces.append(swapped(jnp.concatenate([packed, sib]), "pair", 0))
        else:
            far_pieces.append(swapped(sib, "pair", 0))
        product = raw_product(located, row_sq, sib, dim) / math.sqrt(sib.shape[0])
        results.append(product)
        grams.append(gram_of(product))
        cluster = jnp.concatenate([cluster, sib])
    far_total = None
    far_rows = 0
    for piece in far_pieces:
        part = raw_product(located, row_sq, piece, dim)
        far_total = part if far_total is None else far_total + part
        far_rows += piece.shape[0]
    product = far_total / math.sqrt(far_rows)
    results.append(product)
    grams.append(gram_of(product))
    n_tiers = len(grams)
    done = [grams[0]]
    for tier_num in range(1, n_tiers - 1):
        if tier_num == n_tiers - 2:
            break
        local = grams[tier_num]
        for bit_num in range(tier_num):
            local = local + swapped(local, "leaf", bit_num)
        done.append(local)
    tail = jnp.stack(grams[n_tiers - 2:])
    for bit_num in range(n_tiers - 2):
        tail = tail + swapped(tail, "leaf", bit_num)
    last = tail[1] + swapped(tail[1], "leaf", n_tiers - 2)
    done.extend([tail[0], last])
    stacked = jnp.stack(done)
    divisors = jnp.asarray(
        [float((1 << tier_num) * rows_n) for tier_num in range(len(grams))], jnp.float32
    )
    stacked = stacked / divisors[:, None, None]
    return (jnp.concatenate(results, axis=1), stacked[None])


def solution(mesh):
    n_leaf = mesh.shape["leaf"]
    n_level = mesh.shape["level"]
    fine = Mesh(mesh.devices.reshape(n_leaf, n_level // 2, 2), ("leaf", "lvl", "pair"))
    axes = ("leaf", "lvl", "pair")
    in_specs = (P(axes, None), P(axes, None), P(axes, None))
    out_specs = (P(axes, None), P(axes, None, None, None))
    return jax.shard_map(
        per_device, mesh=fine, in_specs=in_specs, out_specs=out_specs, check_vma=False
    )
```

```python
import math

import jax
import jax.numpy as jnp
from jax import lax
from jax.sharding import Mesh, PartitionSpec as P


def swapped(value, axis, stride):
    mask = 2**stride
    pairs = [(source, source ^ mask) for source in range(lax.axis_size(axis))]
    return lax.ppermute(value, axis, pairs)


def squares_of(coords):
    return jnp.sum(jnp.square(coords.astype(jnp.float32)), axis=-1)


def raw_product(row_pts, row_sq, cols, dim):
    col_pts = cols[:, :dim]
    col_sketch = cols[:, dim:]
    col_sq = squares_of(col_pts)
    cross = lax.dot_general(
        row_pts, col_pts, (((1,), (1,)), ((), ())), preferred_element_type=jnp.float32
    )
    distance = row_sq[:, None] + col_sq[None, :] - 2.0 * cross
    kernel = jnp.exp((2.0 * dim - distance) * (2.0 / dim)).astype(jnp.bfloat16)
    return jnp.dot(kernel, col_sketch, preferred_element_type=jnp.float32)


def gram_of(product):
    return jnp.dot(
        product.T, product, precision=lax.Precision.HIGHEST, preferred_element_type=jnp.float32
    )


def per_device(points, sketch_matrix, leaf_order):
    dim = points.shape[1]
    rows_n = points.shape[0]
    picks = leaf_order[0][:, None] == jnp.arange(rows_n, dtype=leaf_order.dtype)[None, :]
    located = jnp.dot(
        picks.astype(points.dtype), points, preferred_element_type=jnp.float32
    ).astype(points.dtype)
    row_sq = squares_of(located)
    packed = jnp.concatenate([located, sketch_matrix], axis=1)
    leaf_bits = lax.axis_size("leaf").bit_length() - 1
    top = leaf_bits - 1
    y_rows = swapped(located, "leaf", top)
    y_sq = squares_of(y_rows)
    cluster = packed
    other_pieces = []
    results = []
    grams = []
    for tier_num in range(top):
        sib = swapped(cluster, "leaf", tier_num)
        if tier_num == 0:
            other_pieces.append(swapped(jnp.concatenate([packed, sib]), "pair", 0))
        else:
            other_pieces.append(swapped(sib, "pair", 0))
        product = raw_product(located, row_sq, sib, dim) / math.sqrt(sib.shape[0])
        results.append(product)
        grams.append(gram_of(product))
        cluster = jnp.concatenate([cluster, sib])
    partner_near = raw_product(y_rows, y_sq, cluster, dim)
    partner_far = None
    for piece in other_pieces:
        part = raw_product(y_rows, y_sq, piece, dim)
        partner_far = part if partner_far is None else partner_far + part
    back = swapped(jnp.stack([partner_near, partner_far]), "leaf", top)
    product = back[0] / math.sqrt(cluster.shape[0])
    results.append(product)
    grams.append(gram_of(product))
    own_far = None
    far_rows = 0
    for piece in other_pieces:
        part = raw_product(located, row_sq, piece, dim)
        own_far = part if own_far is None else own_far + part
        far_rows += piece.shape[0]
    product = (own_far + back[1]) / math.sqrt(2 * far_rows)
    results.append(product)
    grams.append(gram_of(product))
    n_tiers = len(grams)
    done = [grams[0]]
    for tier_num in range(1, n_tiers - 1):
        if tier_num == n_tiers - 2:
            break
        local = grams[tier_num]
        for bit_num in range(tier_num):
            local = local + swapped(local, "leaf", bit_num)
        done.append(local)
    tail = jnp.stack(grams[n_tiers - 2:])
    for bit_num in range(n_tiers - 2):
        tail = tail + swapped(tail, "leaf", bit_num)
    last = tail[1] + swapped(tail[1], "leaf", n_tiers - 2)
    done.extend([tail[0], last])
    stacked = jnp.stack(done)
    divisors = jnp.asarray(
        [float((1 << tier_num) * rows_n) for tier_num in range(len(grams))], jnp.float32
    )
    stacked = stacked / divisors[:, None, None]
    return (jnp.concatenate(results, axis=1), stacked[None])


def solution(mesh):
    n_leaf = mesh.shape["leaf"]
    n_level = mesh.shape["level"]
    fine = Mesh(mesh.devices.reshape(n_leaf, n_level // 2, 2), ("leaf", "lvl", "pair"))
    axes = ("leaf", "lvl", "pair")
    in_specs = (P(axes, None), P(axes, None), P(axes, None))
    out_specs = (P(axes, None), P(axes, None, None, None))
    return jax.shard_map(
        per_device, mesh=fine, in_specs=in_specs, out_specs=out_specs, check_vma=False
    )
```

```python
import math

import jax
import jax.numpy as jnp
from jax import lax
from jax.sharding import Mesh, PartitionSpec as P


def swapped(value, axis, stride):
    mask = 2**stride
    pairs = [(source, source ^ mask) for source in range(lax.axis_size(axis))]
    return lax.ppermute(value, axis, pairs)


def squares_of(coords):
    return jnp.sum(jnp.square(coords.astype(jnp.float32)), axis=-1)


def raw_product(row_pts, row_sq, cols, dim):
    col_pts = cols[:, :dim]
    col_sketch = cols[:, dim:]
    col_sq = squares_of(col_pts)
    cross = lax.dot_general(
        row_pts, col_pts, (((1,), (1,)), ((), ())), preferred_element_type=jnp.float32
    )
    distance = row_sq[:, None] + col_sq[None, :] - 2.0 * cross
    kernel = jnp.exp((2.0 * dim - distance) * (2.0 / dim)).astype(jnp.bfloat16)
    return jnp.dot(kernel, col_sketch, preferred_element_type=jnp.float32)


def gram_of(product):
    return jnp.dot(
        product.T, product, precision=lax.Precision.HIGHEST, preferred_element_type=jnp.float32
    )


def per_device(points, sketch_matrix, leaf_order):
    dim = points.shape[1]
    rows_n = points.shape[0]
    picks = leaf_order[0][:, None] == jnp.arange(rows_n, dtype=leaf_order.dtype)[None, :]
    located = jnp.dot(
        picks.astype(points.dtype), points, preferred_element_type=jnp.float32
    ).astype(points.dtype)
    row_sq = squares_of(located)
    packed = jnp.concatenate([located, sketch_matrix], axis=1)
    leaf_bits = lax.axis_size("leaf").bit_length() - 1
    top = leaf_bits - 1
    y_rows = swapped(located, "leaf", top)
    y_sq = squares_of(y_rows)
    cluster = packed
    other_pieces = []
    results = []
    grams = []
    partner_near = None
    for tier_num in range(top):
        sib = swapped(cluster, "leaf", tier_num)
        if tier_num == 0:
            first = jnp.concatenate([packed, sib])
            other_pieces.append(swapped(first, "pair", 0))
            partner_near = raw_product(y_rows, y_sq, first, dim)
        else:
            other_pieces.append(swapped(sib, "pair", 0))
            partner_near = partner_near + raw_product(y_rows, y_sq, sib, dim)
        product = raw_product(located, row_sq, sib, dim) / math.sqrt(sib.shape[0])
        results.append(product)
        grams.append(gram_of(product))
        cluster = jnp.concatenate([cluster, sib])
    partner_far = None
    for piece in other_pieces:
        part = raw_product(y_rows, y_sq, piece, dim)
        partner_far = part if partner_far is None else partner_far + part
    back = swapped(jnp.stack([partner_near, partner_far]), "leaf", top)
    product = back[0] / math.sqrt(cluster.shape[0])
    results.append(product)
    grams.append(gram_of(product))
    own_far = None
    far_rows = 0
    for piece in other_pieces:
        part = raw_product(located, row_sq, piece, dim)
        own_far = part if own_far is None else own_far + part
        far_rows += piece.shape[0]
    product = (own_far + back[1]) / math.sqrt(2 * far_rows)
    results.append(product)
    grams.append(gram_of(product))
    n_tiers = len(grams)
    done = [grams[0]]
    for tier_num in range(1, n_tiers - 1):
        if tier_num == n_tiers - 2:
            break
        local = grams[tier_num]
        for bit_num in range(tier_num):
            local = local + swapped(local, "leaf", bit_num)
        done.append(local)
    tail = jnp.stack(grams[n_tiers - 2:])
    for bit_num in range(n_tiers - 2):
        tail = tail + swapped(tail, "leaf", bit_num)
    last = tail[1] + swapped(tail[1], "leaf", n_tiers - 2)
    done.extend([tail[0], last])
    stacked = jnp.stack(done)
    divisors = jnp.asarray(
        [float((1 << tier_num) * rows_n) for tier_num in range(len(grams))], jnp.float32
    )
    stacked = stacked / divisors[:, None, None]
    return (jnp.concatenate(results, axis=1), stacked[None])


def solution(mesh):
    n_leaf = mesh.shape["leaf"]
    n_level = mesh.shape["level"]
    fine = Mesh(mesh.devices.reshape(n_leaf, n_level // 2, 2), ("leaf", "lvl", "pair"))
    axes = ("leaf", "lvl", "pair")
    in_specs = (P(axes, None), P(axes, None), P(axes, None))
    out_specs = (P(axes, None), P(axes, None, None, None))
    return jax.shard_map(
        per_device, mesh=fine, in_specs=in_specs, out_specs=out_specs, check_vma=False
    )
```

```python
import math

import jax
import jax.numpy as jnp
from jax import lax
from jax.sharding import Mesh, PartitionSpec as P


def swapped(value, axis, stride):
    return exchanged(value, axis, 2**stride)


def exchanged(value, axis, mask):
    pairs = [(source, source ^ mask) for source in range(lax.axis_size(axis))]
    return lax.ppermute(value, axis, pairs)


def squares_of(coords):
    return jnp.sum(jnp.square(coords.astype(jnp.float32)), axis=-1)


def raw_product(row_pts, row_sq, cols, dim):
    col_pts = cols[:, :dim]
    col_sketch = cols[:, dim:]
    col_sq = squares_of(col_pts)
    cross = lax.dot_general(
        row_pts, col_pts, (((1,), (1,)), ((), ())), preferred_element_type=jnp.float32
    )
    distance = row_sq[:, None] + col_sq[None, :] - 2.0 * cross
    kernel = jnp.exp((2.0 * dim - distance) * (2.0 / dim)).astype(jnp.bfloat16)
    return jnp.dot(kernel, col_sketch, preferred_element_type=jnp.float32)


def gram_of(product):
    return jnp.dot(
        product.T, product, precision=lax.Precision.HIGHEST, preferred_element_type=jnp.float32
    )


def per_device(points, sketch_matrix, leaf_order):
    dim = points.shape[1]
    rows_n = points.shape[0]
    picks = leaf_order[0][:, None] == jnp.arange(rows_n, dtype=leaf_order.dtype)[None, :]
    located = jnp.dot(
        picks.astype(points.dtype), points, preferred_element_type=jnp.float32
    ).astype(points.dtype)
    row_sq = squares_of(located)
    packed = jnp.concatenate([located, sketch_matrix], axis=1)
    leaf_bits = lax.axis_size("leaf").bit_length() - 1
    top = leaf_bits - 1
    y_rows = swapped(located, "leaf", top)
    y_sq = squares_of(y_rows)
    cluster = [packed]
    other_pieces = []
    results = []
    grams = []
    for tier_num in range(top):
        sibs = [exchanged(packed, "leaf", mask) for mask in range(1 << tier_num, 2 << tier_num)]
        sib = jnp.concatenate(sibs) if len(sibs) > 1 else sibs[0]
        if tier_num == 0:
            other_pieces.append(swapped(jnp.concatenate([packed, sib]), "pair", 0))
        else:
            other_pieces.append(swapped(sib, "pair", 0))
        product = raw_product(located, row_sq, sib, dim) / math.sqrt(sib.shape[0])
        results.append(product)
        grams.append(gram_of(product))
        cluster.append(sib)
    cluster = jnp.concatenate(cluster)
    partner_near = raw_product(y_rows, y_sq, cluster, dim)
    partner_far = None
    for piece in other_pieces:
        part = raw_product(y_rows, y_sq, piece, dim)
        partner_far = part if partner_far is None else partner_far + part
    back = swapped(jnp.concatenate([partner_near, partner_far], axis=1), "leaf", top)
    rank = partner_near.shape[1]
    product = back[:, :rank] / math.sqrt(cluster.shape[0])
    results.append(product)
    grams.append(gram_of(product))
    own_far = None
    far_rows = 0
    for piece in other_pieces:
        part = raw_product(located, row_sq, piece, dim)
        own_far = part if own_far is None else own_far + part
        far_rows += piece.shape[0]
    product = (own_far + back[:, rank:]) / math.sqrt(2 * far_rows)
    results.append(product)
    grams.append(gram_of(product))
    n_tiers = len(grams)
    done = [grams[0]]
    for tier_num in range(1, n_tiers - 1):
        if tier_num == n_tiers - 2:
            break
        local = grams[tier_num]
        for bit_num in range(tier_num):
            local = local + swapped(local, "leaf", bit_num)
        done.append(local)
    tail = jnp.stack(grams[n_tiers - 2:])
    for bit_num in range(n_tiers - 2):
        tail = tail + swapped(tail, "leaf", bit_num)
    last = tail[1] + swapped(tail[1], "leaf", n_tiers - 2)
    done.extend([tail[0], last])
    stacked = jnp.stack(done)
    divisors = jnp.asarray(
        [float((1 << tier_num) * rows_n) for tier_num in range(len(grams))], jnp.float32
    )
    stacked = stacked / divisors[:, None, None]
    return (jnp.concatenate(results, axis=1), stacked[None])


def solution(mesh):
    n_leaf = mesh.shape["leaf"]
    n_level = mesh.shape["level"]
    fine = Mesh(mesh.devices.reshape(n_leaf, n_level // 2, 2), ("leaf", "lvl", "pair"))
    axes = ("leaf", "lvl", "pair")
    in_specs = (P(axes, None), P(axes, None), P(axes, None))
    out_specs = (P(axes, None), P(axes, None, None, None))
    return jax.shard_map(
        per_device, mesh=fine, in_specs=in_specs, out_specs=out_specs, check_vma=False
    )
```

```python
import math

import jax
import jax.numpy as jnp
from jax import lax
from jax.sharding import Mesh, PartitionSpec as P


def swapped(value, axis, stride):
    return exchanged(value, axis, 2**stride)


def exchanged(value, axis, mask):
    pairs = [(source, source ^ mask) for source in range(lax.axis_size(axis))]
    return lax.ppermute(value, axis, pairs)


def squares_of(coords):
    return jnp.sum(jnp.square(coords.astype(jnp.float32)), axis=-1)


def raw_product(row_pts, row_sq, cols, dim):
    col_pts = cols[:, :dim]
    col_sketch = cols[:, dim:]
    col_sq = squares_of(col_pts)
    cross = lax.dot_general(
        row_pts, col_pts, (((1,), (1,)), ((), ())), preferred_element_type=jnp.float32
    )
    distance = row_sq[:, None] + col_sq[None, :] - 2.0 * cross
    kernel = jnp.exp((2.0 * dim - distance) * (2.0 / dim)).astype(jnp.bfloat16)
    return jnp.dot(kernel, col_sketch, preferred_element_type=jnp.float32)


def gram_of(product):
    return jnp.dot(
        product.T, product, precision=lax.Precision.HIGHEST, preferred_element_type=jnp.float32
    )


def device_body(points, sketch_matrix, leaf_order):
    dim = points.shape[1]
    rows_n = points.shape[0]
    picks = leaf_order[0][:, None] == jnp.arange(rows_n, dtype=leaf_order.dtype)[None, :]
    located = jnp.dot(
        picks.astype(points.dtype), points, preferred_element_type=jnp.float32
    ).astype(points.dtype)
    row_sq = squares_of(located)
    packed = jnp.concatenate([located, sketch_matrix], axis=1)
    leaf_bits = lax.axis_size("leaf").bit_length() - 1
    top = leaf_bits - 1
    y_rows = swapped(located, "leaf", top)
    y_sq = squares_of(y_rows)
    cluster = [packed]
    other_pieces = []
    results = []
    grams = []
    for tier_num in range(top):
        sibs = [exchanged(packed, "leaf", mask) for mask in range(1 << tier_num, 2 << tier_num)]
        sib = jnp.concatenate(sibs) if len(sibs) > 1 else sibs[0]
        product = raw_product(located, row_sq, sib, dim) / math.sqrt(sib.shape[0])
        results.append(product)
        grams.append(gram_of(product))
        cluster.append(sib)
    cluster = jnp.concatenate(cluster)
    other_pieces = [swapped(cluster, "pair", 0)]
    partner_near = raw_product(y_rows, y_sq, cluster, dim)
    partner_far = None
    for piece in other_pieces:
        part = raw_product(y_rows, y_sq, piece, dim)
        partner_far = part if partner_far is None else partner_far + part
    back = swapped(jnp.concatenate([partner_near, partner_far], axis=1), "leaf", top)
    rank = partner_near.shape[1]
    product = back[:, :rank] / math.sqrt(cluster.shape[0])
    results.append(product)
    grams.append(gram_of(product))
    own_far = None
    far_rows = 0
    for piece in other_pieces:
        part = lax.optimization_barrier(raw_product(located, row_sq, piece, dim))
        own_far = part if own_far is None else own_far + part
        far_rows += piece.shape[0]
    product = (own_far + back[:, rank:]) / math.sqrt(2 * far_rows)
    results.append(product)
    grams.append(gram_of(product))
    n_tiers = len(grams)
    done = [grams[0]]
    for tier_num in range(1, n_tiers - 1):
        if tier_num == n_tiers - 2:
            break
        local = grams[tier_num]
        for bit_num in range(tier_num):
            local = local + swapped(local, "leaf", bit_num)
        done.append(local)
    tail = jnp.stack(grams[n_tiers - 2:])
    for bit_num in range(n_tiers - 2):
        tail = tail + swapped(tail, "leaf", bit_num)
    last = tail[1] + swapped(tail[1], "leaf", n_tiers - 2)
    done.extend([tail[0], last])
    stacked = jnp.stack(done)
    divisors = jnp.asarray(
        [float((1 << tier_num) * rows_n) for tier_num in range(len(grams))], jnp.float32
    )
    stacked = stacked / divisors[:, None, None]
    return (jnp.concatenate(results, axis=1), stacked[None])


def solution(mesh):
    n_leaf = mesh.shape["leaf"]
    n_level = mesh.shape["level"]
    fine = Mesh(mesh.devices.reshape(n_leaf, n_level // 2, 2), ("leaf", "lvl", "pair"))
    axes = ("leaf", "lvl", "pair")
    in_specs = (P(axes, None), P(axes, None), P(axes, None))
    out_specs = (P(axes, None), P(axes, None, None, None))
    return jax.shard_map(
        device_body, mesh=fine, in_specs=in_specs, out_specs=out_specs, check_vma=False
    )
```

```python
import math

import jax
import jax.numpy as jnp
from jax import lax
from jax.sharding import Mesh, PartitionSpec as P


def swapped(value, axis, stride):
    return exchanged(value, axis, 2**stride)


def exchanged(value, axis, mask):
    pairs = [(source, source ^ mask) for source in range(lax.axis_size(axis))]
    return lax.ppermute(value, axis, pairs)


def squares_of(coords):
    return jnp.sum(jnp.square(coords.astype(jnp.float32)), axis=-1)


def raw_product(row_pts, row_sq, cols, dim):
    col_pts = cols[:, :dim]
    col_sketch = cols[:, dim:]
    col_sq = squares_of(col_pts)
    cross = lax.dot_general(
        row_pts, col_pts, (((1,), (1,)), ((), ())), preferred_element_type=jnp.float32
    )
    distance = row_sq[:, None] + col_sq[None, :] - 2.0 * cross
    kernel = jnp.exp((2.0 * dim - distance) * (2.0 / dim)).astype(jnp.bfloat16)
    return jnp.dot(kernel, col_sketch, preferred_element_type=jnp.float32)


def gram_of(product):
    return jnp.dot(
        product.T, product, precision=lax.Precision.HIGHEST, preferred_element_type=jnp.float32
    )


def device_body(points, sketch_matrix, leaf_order):
    dim = points.shape[1]
    rows_n = points.shape[0]
    picks = leaf_order[0][:, None] == jnp.arange(rows_n, dtype=leaf_order.dtype)[None, :]
    located = jnp.dot(
        picks.astype(points.dtype), points, preferred_element_type=jnp.float32
    ).astype(points.dtype)
    row_sq = squares_of(located)
    packed = jnp.concatenate([located, sketch_matrix], axis=1)
    leaf_bits = lax.axis_size("leaf").bit_length() - 1
    top = leaf_bits - 1
    y_rows = swapped(located, "leaf", top)
    y_sq = squares_of(y_rows)
    cluster = [packed]
    other_pieces = []
    results = []
    grams = []
    for tier_num in range(top):
        sibs = [exchanged(packed, "leaf", mask) for mask in range(1 << tier_num, 2 << tier_num)]
        sib = jnp.concatenate(sibs) if len(sibs) > 1 else sibs[0]
        product = raw_product(located, row_sq, sib, dim) / math.sqrt(sib.shape[0])
        results.append(product)
        grams.append(gram_of(product))
        cluster.append(sib)
    cluster = jnp.concatenate(cluster)
    other_pieces = [swapped(cluster, "pair", 0)]
    partner_near = raw_product(y_rows, y_sq, cluster, dim)
    partner_far = None
    for piece in other_pieces:
        part = raw_product(y_rows, y_sq, piece, dim)
        partner_far = part if partner_far is None else partner_far + part
    back = swapped(jnp.concatenate([partner_near, partner_far], axis=1), "leaf", top)
    rank = partner_near.shape[1]
    product = back[:, :rank] / math.sqrt(cluster.shape[0])
    results.append(product)
    grams.append(gram_of(product))
    own_far = None
    far_rows = 0
    for piece in other_pieces:
        part = lax.optimization_barrier(raw_product(located, row_sq, piece, dim))
        own_far = part if own_far is None else own_far + part
        far_rows += piece.shape[0]
    product = (own_far + back[:, rank:]) / math.sqrt(2 * far_rows)
    results.append(product)
    grams.append(gram_of(product))
    n_tiers = len(grams)
    first = jnp.stack(grams[1:])
    first = first + swapped(first, "leaf", 0)
    tail = first[1:]
    for bit_num in range(1, n_tiers - 2):
        tail = tail + swapped(tail, "leaf", bit_num)
    last = tail[-1] + swapped(tail[-1], "leaf", n_tiers - 2)
    done = [grams[0], first[0], tail[0], last]
    stacked = jnp.stack(done)
    divisors = jnp.asarray(
        [float((1 << tier_num) * rows_n) for tier_num in range(len(grams))], jnp.float32
    )
    stacked = stacked / divisors[:, None, None]
    return (jnp.concatenate(results, axis=1), stacked[None])


def solution(mesh):
    n_leaf = mesh.shape["leaf"]
    n_level = mesh.shape["level"]
    fine = Mesh(mesh.devices.reshape(n_leaf, n_level // 2, 2), ("leaf", "lvl", "pair"))
    axes = ("leaf", "lvl", "pair")
    in_specs = (P(axes, None), P(axes, None), P(axes, None))
    out_specs = (P(axes, None), P(axes, None, None, None))
    return jax.shard_map(
        device_body, mesh=fine, in_specs=in_specs, out_specs=out_specs, check_vma=False
    )
```

```python
import math

import jax
import jax.numpy as jnp
from jax import lax
from jax.sharding import Mesh, PartitionSpec as P


def swapped(value, axis, stride):
    return exchanged(value, axis, 2**stride)


def exchanged(value, axis, mask):
    pairs = [(source, source ^ mask) for source in range(lax.axis_size(axis))]
    return lax.ppermute(value, axis, pairs)


def squares_of(coords):
    return jnp.sum(jnp.square(coords.astype(jnp.float32)), axis=-1)


def raw_product(row_pts, row_sq, cols, dim):
    col_pts = cols[:, :dim]
    col_sketch = cols[:, dim:]
    col_sq = squares_of(col_pts)
    cross = lax.dot_general(
        row_pts, col_pts, (((1,), (1,)), ((), ())), preferred_element_type=jnp.float32
    )
    distance = row_sq[:, None] + col_sq[None, :] - 2.0 * cross
    kernel = jnp.exp((2.0 * dim - distance) * (2.0 / dim)).astype(jnp.bfloat16)
    return jnp.dot(kernel, col_sketch, preferred_element_type=jnp.float32)


def gram_of(product):
    return jnp.dot(
        product.T, product, precision=lax.Precision.HIGHEST, preferred_element_type=jnp.float32
    )


def device_body(points, sketch_matrix, leaf_order):
    dim = points.shape[1]
    rows_n = points.shape[0]
    picks = leaf_order[0][:, None] == jnp.arange(rows_n, dtype=leaf_order.dtype)[None, :]
    located = jnp.dot(
        picks.astype(points.dtype), points, preferred_element_type=jnp.float32
    ).astype(points.dtype)
    row_sq = squares_of(located)
    packed = jnp.concatenate([located, sketch_matrix], axis=1)
    leaf_bits = lax.axis_size("leaf").bit_length() - 1
    top = leaf_bits - 1
    y_rows = swapped(located, "leaf", top)
    y_sq = squares_of(y_rows)
    cluster = [packed]
    other_pieces = []
    results = []
    grams = []
    for tier_num in range(top):
        sibs = [
            exchanged(packed, "leaf", mask) for mask in range(1 << tier_num, 2 << tier_num)
        ]
        sib = jnp.concatenate(sibs) if len(sibs) > 1 else sibs[0]
        product = raw_product(located, row_sq, sib, dim) / math.sqrt(sib.shape[0])
        results.append(product)
        grams.append(gram_of(product))
        cluster.append(sib)
    cluster = jnp.concatenate(cluster)
    other_pieces = [swapped(cluster, "pair", 0)]
    partner_near = raw_product(y_rows, y_sq, cluster, dim)
    partner_far = None
    for piece in other_pieces:
        part = raw_product(y_rows, y_sq, piece, dim)
        partner_far = part if partner_far is None else partner_far + part
    back = swapped(jnp.concatenate([partner_near, partner_far], axis=1), "leaf", top)
    rank = partner_near.shape[1]
    product = back[:, :rank] / math.sqrt(cluster.shape[0])
    results.append(product)
    grams.append(gram_of(product))
    own_far = None
    far_rows = 0
    for piece in other_pieces:
        part = lax.optimization_barrier(raw_product(located, row_sq, piece, dim))
        own_far = part if own_far is None else own_far + part
        far_rows += piece.shape[0]
    product = (own_far + back[:, rank:]) / math.sqrt(2 * far_rows)
    results.append(product)
    grams.append(gram_of(product))
    low = 1 << top
    pair_sum = grams[1]
    quad_sum = [grams[2], grams[3]]
    for mask in range(1, low):
        if mask == 1:
            got = exchanged(jnp.stack(grams[1:]), "leaf", mask)
            pair_sum = pair_sum + got[0]
            got = got[1:]
        else:
            got = exchanged(jnp.stack(grams[2:]), "leaf", mask)
        quad_sum = [quad_sum[0] + got[0], quad_sum[1] + got[1]]
    last = quad_sum[1] + exchanged(quad_sum[1], "leaf", low)
    done = [grams[0], pair_sum, quad_sum[0], last]
    stacked = jnp.stack(done)
    divisors = jnp.asarray(
        [float((1 << tier_num) * rows_n) for tier_num in range(len(grams))], jnp.float32
    )
    stacked = stacked / divisors[:, None, None]
    return (jnp.concatenate(results, axis=1), stacked[None])


def solution(mesh):
    n_leaf = mesh.shape["leaf"]
    n_level = mesh.shape["level"]
    fine = Mesh(mesh.devices.reshape(n_leaf, n_level // 2, 2), ("leaf", "lvl", "pair"))
    axes = ("leaf", "lvl", "pair")
    in_specs = (P(axes, None), P(axes, None), P(axes, None))
    out_specs = (P(axes, None), P(axes, None, None, None))
    return jax.shard_map(
        device_body, mesh=fine, in_specs=in_specs, out_specs=out_specs, check_vma=False
    )
```

```python
import math

import jax
import jax.numpy as jnp
from jax import lax
from jax.sharding import Mesh, PartitionSpec as P


def swapped(value, axis, stride):
    return exchanged(value, axis, 2**stride)


def exchanged(value, axis, mask):
    pairs = [(source, source ^ mask) for source in range(lax.axis_size(axis))]
    return lax.ppermute(value, axis, pairs)


def squares_of(coords):
    return jnp.sum(jnp.square(coords.astype(jnp.float32)), axis=-1)


def raw_product(row_pts, row_sq, cols, dim):
    col_pts = cols[:, :dim]
    col_sketch = cols[:, dim:]
    col_sq = squares_of(col_pts)
    cross = lax.dot_general(
        row_pts, col_pts, (((1,), (1,)), ((), ())), preferred_element_type=jnp.float32
    )
    distance = row_sq[:, None] + col_sq[None, :] - 2.0 * cross
    kernel = jnp.exp((2.0 * dim - distance) * (2.0 / dim)).astype(jnp.bfloat16)
    return jnp.dot(kernel, col_sketch, preferred_element_type=jnp.float32)


def gram_of(product):
    return jnp.dot(
        product.T, product, precision=lax.Precision.HIGHEST, preferred_element_type=jnp.float32
    )


def device_body(points, sketch_matrix, leaf_order):
    dim = points.shape[1]
    rows_n = points.shape[0]
    picks = leaf_order[0][:, None] == jnp.arange(rows_n, dtype=leaf_order.dtype)[None, :]
    located = jnp.dot(
        picks.astype(points.dtype), points, preferred_element_type=jnp.float32
    ).astype(points.dtype)
    row_sq = squares_of(located)
    packed = jnp.concatenate([located, sketch_matrix], axis=1)
    leaf_bits = lax.axis_size("leaf").bit_length() - 1
    top = leaf_bits - 1
    y_rows = swapped(located, "leaf", top)
    y_sq = squares_of(y_rows)
    cluster = [packed]
    other_pieces = []
    results = []
    grams = []
    for tier_num in range(top):
        sibs = [exchanged(packed, "leaf", mask) for mask in range(1 << tier_num, 2 << tier_num)]
        sib = jnp.concatenate(sibs) if len(sibs) > 1 else sibs[0]
        product = raw_product(located, row_sq, sib, dim) / math.sqrt(sib.shape[0])
        results.append(product)
        grams.append(gram_of(product))
        cluster.append(sib)
    cluster = jnp.concatenate(cluster)
    other_pieces = [swapped(cluster, "pair", 0)]
    partner_near = raw_product(y_rows, y_sq, cluster, dim)
    partner_far = None
    for piece in other_pieces:
        part = raw_product(y_rows, y_sq, piece, dim)
        partner_far = part if partner_far is None else partner_far + part
    back = swapped(jnp.concatenate([partner_near, partner_far], axis=1), "leaf", top)
    rank = partner_near.shape[1]
    product = back[:, :rank] / math.sqrt(cluster.shape[0])
    results.append(product)
    grams.append(gram_of(product))
    own_far = None
    far_rows = 0
    for piece in other_pieces:
        part = lax.optimization_barrier(raw_product(located, row_sq, piece, dim))
        own_far = part if own_far is None else own_far + part
        far_rows += piece.shape[0]
    far_back = swapped(own_far, "leaf", top)
    product = (own_far + back[:, rank:]) / math.sqrt(2 * far_rows)
    results.append(product)
    mirror = (far_back + partner_far) / math.sqrt(2 * far_rows)
    grams.append(gram_of(product) + gram_of(mirror))
    low = 1 << top
    pair_sum = grams[1]
    quad_sum = [grams[2], grams[3]]
    for mask in range(1, low):
        if mask == 1:
            got = exchanged(jnp.stack(grams[1:]), "leaf", mask)
            pair_sum = pair_sum + got[0]
            got = got[1:]
        else:
            got = exchanged(jnp.stack(grams[2:]), "leaf", mask)
        quad_sum = [quad_sum[0] + got[0], quad_sum[1] + got[1]]
    done = [grams[0], pair_sum, quad_sum[0], quad_sum[1]]
    stacked = jnp.stack(done)
    divisors = jnp.asarray(
        [float((1 << tier_num) * rows_n) for tier_num in range(len(grams))], jnp.float32
    )
    stacked = stacked / divisors[:, None, None]
    return (jnp.concatenate(results, axis=1), stacked[None])


def solution(mesh):
    n_leaf = mesh.shape["leaf"]
    n_level = mesh.shape["level"]
    fine = Mesh(mesh.devices.reshape(n_leaf, n_level // 2, 2), ("leaf", "lvl", "pair"))
    axes = ("leaf", "lvl", "pair")
    in_specs = (P(axes, None), P(axes, None), P(axes, None))
    out_specs = (P(axes, None), P(axes, None, None, None))
    return jax.shard_map(
        device_body, mesh=fine, in_specs=in_specs, out_specs=out_specs, check_vma=False
    )
```

```python
import math

import jax
import jax.numpy as jnp
from jax import lax
from jax.sharding import Mesh, PartitionSpec as P


def swapped(value, axis, stride):
    return exchanged(value, axis, 2**stride)


def exchanged(value, axis, mask):
    pairs = [(source, source ^ mask) for source in range(lax.axis_size(axis))]
    return lax.ppermute(value, axis, pairs)


def squares_of(coords):
    return jnp.sum(jnp.square(coords.astype(jnp.float32)), axis=-1)


def raw_product(row_pts, row_sq, cols, dim):
    col_pts = cols[:, :dim]
    col_sketch = cols[:, dim:]
    col_sq = squares_of(col_pts)
    cross = lax.dot_general(
        row_pts, col_pts, (((1,), (1,)), ((), ())), preferred_element_type=jnp.float32
    )
    distance = row_sq[:, None] + col_sq[None, :] - 2.0 * cross
    kernel = jnp.exp((2.0 * dim - distance) * (2.0 / dim)).astype(jnp.bfloat16)
    return jnp.dot(kernel, col_sketch, preferred_element_type=jnp.float32)


def gram_of(product):
    return jnp.dot(
        product.T, product, precision=lax.Precision.HIGHEST, preferred_element_type=jnp.float32
    )


def device_body(points, sketch_matrix, leaf_order):
    dim = points.shape[1]
    rows_n = points.shape[0]
    picks = leaf_order[0][:, None] == jnp.arange(rows_n, dtype=leaf_order.dtype)[None, :]
    located = jnp.dot(
        picks.astype(points.dtype), points, preferred_element_type=jnp.float32
    ).astype(points.dtype)
    row_sq = squares_of(located)
    packed = jnp.concatenate([located, sketch_matrix], axis=1)
    leaf_bits = lax.axis_size("leaf").bit_length() - 1
    top = leaf_bits - 1
    y_rows = swapped(located, "leaf", top)
    y_sq = squares_of(y_rows)
    partner_own = lax.optimization_barrier(raw_product(y_rows, y_sq, packed, dim))
    cluster = [packed]
    other_pieces = []
    results = []
    grams = []
    for tier_num in range(top):
        sibs = [
            exchanged(packed, "leaf", mask) for mask in range(1 << tier_num, 2 << tier_num)
        ]
        sib = jnp.concatenate(sibs) if len(sibs) > 1 else sibs[0]
        product = raw_product(located, row_sq, sib, dim) / math.sqrt(sib.shape[0])
        results.append(product)
        grams.append(gram_of(product))
        cluster.append(sib)
    received = jnp.concatenate(cluster[1:])
    cluster = jnp.concatenate(cluster)
    other_pieces = [swapped(cluster, "pair", 0)]
    partner_near = partner_own + raw_product(y_rows, y_sq, received, dim)
    partner_far = None
    for piece in other_pieces:
        part = raw_product(y_rows, y_sq, piece, dim)
        partner_far = part if partner_far is None else partner_far + part
    back = swapped(jnp.concatenate([partner_near, partner_far], axis=1), "leaf", top)
    rank = partner_near.shape[1]
    product = back[:, :rank] / math.sqrt(cluster.shape[0])
    results.append(product)
    grams.append(gram_of(product))
    own_far = None
    far_rows = 0
    for piece in other_pieces:
        part = lax.optimization_barrier(raw_product(located, row_sq, piece, dim))
        own_far = part if own_far is None else own_far + part
        far_rows += piece.shape[0]
    far_back = swapped(own_far, "leaf", top)
    product = (own_far + back[:, rank:]) / math.sqrt(2 * far_rows)
    results.append(product)
    mirror = (far_back + partner_far) / math.sqrt(2 * far_rows)
    grams.append(gram_of(product) + gram_of(mirror))
    low = 1 << top
    pair_sum = grams[1]
    quad_sum = [grams[2], grams[3]]
    for mask in range(1, low):
        if mask == 1:
            got = exchanged(jnp.stack(grams[1:]), "leaf", mask)
            pair_sum = pair_sum + got[0]
            got = got[1:]
        else:
            got = exchanged(jnp.stack(grams[2:]), "leaf", mask)
        quad_sum = [quad_sum[0] + got[0], quad_sum[1] + got[1]]
    done = [grams[0], pair_sum, quad_sum[0], quad_sum[1]]
    stacked = jnp.stack(done)
    divisors = jnp.asarray(
        [float((1 << tier_num) * rows_n) for tier_num in range(len(grams))], jnp.float32
    )
    stacked = stacked / divisors[:, None, None]
    return (jnp.concatenate(results, axis=1), stacked[None])


def solution(mesh):
    n_leaf = mesh.shape["leaf"]
    n_level = mesh.shape["level"]
    fine = Mesh(mesh.devices.reshape(n_leaf, n_level // 2, 2), ("leaf", "lvl", "pair"))
    axes = ("leaf", "lvl", "pair")
    in_specs = (P(axes, None), P(axes, None), P(axes, None))
    out_specs = (P(axes, None), P(axes, None, None, None))
    return jax.shard_map(
        device_body, mesh=fine, in_specs=in_specs, out_specs=out_specs, check_vma=False
    )
```
